512 devices in a mesh: ctx: 64 (over z, y), exp: 8 (over x, core).
Axes of the slice: x: 4, y: 4, z: 16, core: 2. Of those that a mesh axis runs over, the one named last changes fastest.
Arguments:
- queries: bfloat16 [8, 8192, 2048], P('exp', 'ctx'), may hold values from -64 to 64
- rotated_key_rows: bfloat16 [8, 8192, 256], P('exp', 'ctx'), may hold values from -7 to 7
- value_row_array: bfloat16 [8, 8192, 256], P('exp', 'ctx'), may hold values from -6 to 6
- residual: bfloat16 [8, 8192, 2048], P('exp', 'ctx'), may hold values from -40 to 40
- norm_gain: float32 [2048], replicated, may hold values from 0.1 to 1.9
- expert_ids: int32 [8, 8192, 1], P('exp', 'ctx'), may hold values from 0 to 127; in each aligned block of 128 rows (0 to 127, 128 to 255, ..., all dimensions but the last counted through in order) at most 2 rows name the same one
- gate_values: float32 [8, 8192, 1], P('exp', 'ctx'), may hold values from 0.25 to 1
- w_gate_up: bfloat16 [64, 8, 2, 192, 2048], P('ctx', 'exp'), may hold values from -0.125 to 0.125
- w_down: bfloat16 [64, 8, 192, 2048], P('ctx', 'exp'), may hold values from -0.21875 to 0.21875
Outputs:
- layer_out: bfloat16 [8, 8192, 2048], P('exp', 'ctx')
The draws below stay inside these ranges and needn't reach their ends.
Inputs may be any that keep to these rules, and one draw needn't show every extreme that they name: `expert_ids`: among the rows of one device (aligned blocks of 128 tokens along the second dimension) no expert is named more than 2 times, a bound that some block reaches.
All inputs are finite; a program needn't handle non-finite values.
Results may differ from the reference program's by a relative error of at most 0.013.
Values may be sent and summed in bfloat16 or wider, within the bound.
No kernel may reach another device: no remote copies, remote signals or barrier semaphores. Data moves between devices by JAX's collectives and lax.ppermute only.
A program may use at most 64 MiB of HBM per device.

```python
import math
import jax
import jax.numpy as jnp
import numpy as np
from jax import lax

D = 2048
HID = 768
QUERY_HEADS = 16
KEY_VALUE_HEADS = 2
HEAD_SIZE = 128
TOP = 1
TOK_DEV = 128
EPG = 16
EXPERTS = 128
QUARTER = 192
GROUP_TOKENS = 8192
PROMPT_LENGTH = 4096
MOST = 2
N_CTX = 64
N_EXP = 8


def pair_fields(key):
    query_key = jax.random.fold_in(key, 11)
    keys_random_key = jax.random.fold_in(key, 12)
    key_head_rows = 1.5 * jnp.clip(jax.random.normal(keys_random_key, (N_EXP, GROUP_TOKENS, KEY_VALUE_HEADS, HEAD_SIZE), jnp.float32), -4.0, 4.0)
    query_head_rows = 1.5 * jnp.clip(jax.random.normal(query_key, (N_EXP, GROUP_TOKENS, QUERY_HEADS, HEAD_SIZE), jnp.float32), -4.0, 4.0)
    return (query_head_rows.reshape(N_EXP, GROUP_TOKENS, QUERY_HEADS * HEAD_SIZE), key_head_rows.reshape(N_EXP, GROUP_TOKENS, KEY_VALUE_HEADS * HEAD_SIZE))


def draw_queries(key, part):
    return pair_fields(key)[0].astype(jnp.bfloat16)


def draw_rotated_key_rows(key, part):
    return pair_fields(key)[1].astype(jnp.bfloat16)


def draw_residual(key, part):
    base_key = jax.random.fold_in(key, 21)
    row_key = jax.random.fold_in(key, 22)
    column_key = jax.random.fold_in(key, 23)
    column_scale = jnp.exp(jax.random.uniform(column_key, (1, 1, D), jnp.float32, math.log(0.3), math.log(3.0)))
    row_scale = jnp.exp(jax.random.uniform(row_key, (N_EXP, GROUP_TOKENS, 1), jnp.float32, math.log(0.3), math.log(3.0)))
    base = jnp.clip(jax.random.normal(base_key, (N_EXP, GROUP_TOKENS, D), jnp.float32), -4.0, 4.0)
    return (base * row_scale * column_scale).astype(jnp.bfloat16)


def shard_levels(own_key, extent, pieces, smallest, high):
    gain = 1.0
    for dim, shards_of in pieces:
        steps = jax.random.uniform(jax.random.fold_in(jax.random.fold_in(own_key, 6), dim), (shards_of,), jnp.float32, smallest / len(pieces), high / len(pieces))
        gain = gain * jnp.repeat(jnp.exp(steps), extent[dim] // shards_of).reshape((-1,) + (1,) * (len(extent) - 1 - dim))
    return gain


def assign_block(key, own, number, rows, amount, top, limit, slope):
    order = jax.random.permutation(key, amount)
    crowded, usual = shares(amount, rows * top, limit, slope, True), shares(amount, rows * top, limit, slope, False)
    places = jnp.arange(amount)

    def named(lengths, rotation):
        used = int((lengths > 0).sum())
        fixed = max(1, used // 4)
        moved = fixed + (places - fixed + rotation * (used - fixed)) % max(1, amount - fixed)
        return jnp.zeros((amount,), jnp.int32).at[order[jnp.where(places < fixed, places, moved)]].set(jnp.asarray(lengths, jnp.int32))

    lengths = jnp.where(number % 4 == 0, named(crowded, number // 4), named(usual, number - number // 4 - 1))
    mixed = jax.random.permutation(jax.random.fold_in(own, 3), amount)
    donor, sink = mixed[0:amount // 2 * 2:2], mixed[1:amount // 2 * 2:2]
    room = jnp.minimum(lengths[donor] - 1, limit - lengths[sink]) // 2
    room = jnp.where((donor == order[0]) | (sink == order[0]) | (lengths[sink] == 0), 0, jnp.maximum(room, 0))
    moved = jax.random.randint(jax.random.fold_in(own, 4), (amount // 2,), 0, 1 << 20) % (room + 1)
    lengths = lengths.at[donor].add(-moved).at[sink].add(moved)
    labels = jnp.searchsorted(jnp.cumsum(lengths), jnp.arange(rows * top), side="right").astype(jnp.int32)
    listing = labels.reshape(top, rows).T
    listing = listing[jax.random.permutation(jax.random.fold_in(own, 1), rows)]
    rotation = jax.random.randint(jax.random.fold_in(own, 2), (rows, 1), 0, top)
    return jnp.take_along_axis(listing, (jnp.arange(top)[None, :] + rotation) % top, axis=1)


def shares(amount, total, limit, skew, full):
    weights = [(1 << 20) // math.isqrt(standing ** skew) + 1 for standing in range(1, amount + 1)]
    largest = limit if full else min(limit, max(-(-total // amount), total * weights[0] // sum(weights)))
    least = 1 if total - largest >= amount - 1 else 0
    given, rest = [largest] + [least] * (amount - 1), total - largest - least * (amount - 1)
    while rest > 0:
        candidates = [i for i in range(1, amount) if given[i] < largest] or [i for i in range(1, amount) if given[i] < limit]
        pool, budget = sum([weights[i] for i in candidates]), rest
        for i in candidates:
            extra = min(limit - given[i], max(1, budget * weights[i] // pool), rest)
            given[i] = given[i] + extra
            rest = rest - extra
    return np.array(given)


def scatter_about(rng, extent, deviation, limit, cuts=(), kind=jnp.bfloat16):
    values = deviation * jax.random.normal(rng, extent, jnp.float32)
    if cuts:
        values = values * shard_levels(rng, extent, cuts, -0.22, 0.18)
    return jnp.clip(values, -limit, limit).astype(kind)


def setup_inputs(seed: int = 0) -> dict:
    splits = jax.random.split(jax.random.key(seed), 10)
    queries = draw_queries(jax.random.fold_in(splits[9], 71), 0)
    rotated_key_rows = draw_rotated_key_rows(jax.random.fold_in(splits[9], 71), 0)
    value_row_array = scatter_about(splits[2], (N_EXP, GROUP_TOKENS, KEY_VALUE_HEADS * HEAD_SIZE), 1.0, 6.0, ((0, 8), (1, 64)))
    residual = draw_residual(jax.random.fold_in(splits[9], 71), 0)
    norm_gain = jnp.clip(1.0 + 0.18 * jax.random.normal(splits[4], (D,), jnp.float32), 0.1, 1.9)
    expert_ids_keys = jax.random.split(jax.random.fold_in(splits[5], 1), N_EXP * GROUP_TOKENS // TOK_DEV)
    expert_ids_turns = jax.random.permutation(jax.random.fold_in(splits[5], 3), N_EXP * GROUP_TOKENS // TOK_DEV)
    expert_ids = jax.vmap(lambda own, number: assign_block(jax.random.fold_in(splits[5], 2), own, number, TOK_DEV, EXPERTS, TOP, MOST, 2))(expert_ids_keys, expert_ids_turns).reshape((N_EXP, GROUP_TOKENS, TOP))
    gate_values = jnp.clip(0.25 + 0.75 * jax.random.uniform(splits[6], (N_EXP, GROUP_TOKENS, TOP), jnp.float32) ** shard_levels(splits[6], (N_EXP, GROUP_TOKENS, TOP), ((0, 8), (1, 64)), -0.2, 0.2), 0.25, 1.0)
    w_gate_up = scatter_about(splits[7], (N_CTX, N_EXP, 2, QUARTER, D), D ** -0.5, 0.125, ((0, 64), (1, 8)))
    w_down = scatter_about(splits[8], (N_CTX, N_EXP, QUARTER, D), HID ** -0.5, 0.21875, ((0, 64), (1, 8)))
    return dict(queries=queries, rotated_key_rows=rotated_key_rows, value_row_array=value_row_array, residual=residual, norm_gain=norm_gain, expert_ids=expert_ids, gate_values=gate_values, w_gate_up=w_gate_up, w_down=w_down)


def to_prompts(array):
    width = array.shape[-1]
    split = array.reshape(N_EXP, N_CTX // 2, 2, TOK_DEV, width)
    return jnp.transpose(split, (0, 2, 1, 3, 4)).reshape(N_EXP * 2, PROMPT_LENGTH, width)

def from_prompts(array):
    width = array.shape[-1]
    split = array.reshape(N_EXP, 2, N_CTX // 2, TOK_DEV, width)
    return jnp.transpose(split, (0, 2, 1, 3, 4)).reshape(N_EXP, GROUP_TOKENS, width)

def attend_whole_prompt(operands):
    queries, rotated_key_rows, value_row_array = operands
    queries_per_key_head = QUERY_HEADS // KEY_VALUE_HEADS
    block_length = math.gcd(PROMPT_LENGTH, 512)
    query_head_rows = queries.reshape(PROMPT_LENGTH // block_length, block_length, KEY_VALUE_HEADS, queries_per_key_head, HEAD_SIZE).astype(jnp.float32)
    key_head_rows = rotated_key_rows.reshape(PROMPT_LENGTH, KEY_VALUE_HEADS, HEAD_SIZE).astype(jnp.float32)
    value_head_rows = value_row_array.reshape(PROMPT_LENGTH, KEY_VALUE_HEADS, HEAD_SIZE).astype(jnp.float32)
    key_pos = jnp.arange(PROMPT_LENGTH, dtype=jnp.int32)

    def one_block(pair):
        query_block, block_index = pair
        scores = jnp.einsum('qhgd,khd->hgqk', query_block, key_head_rows) / math.sqrt(HEAD_SIZE)
        query_pos = block_index * block_length + jnp.arange(block_length, dtype=jnp.int32)
        allowed = key_pos[None, :] <= query_pos[:, None]
        scores = jnp.where(allowed, scores, -1e+30)
        row_peak = lax.optimization_barrier(jnp.max(scores, axis=-1, keepdims=True))
        expo_vals = jnp.exp(scores - row_peak)
        row_total = lax.optimization_barrier(jnp.sum(expo_vals, axis=-1))
        rounded = lax.optimization_barrier(expo_vals.astype(jnp.bfloat16))
        weights = rounded.astype(jnp.float32)
        summed = jnp.einsum('hgqk,khd->qhgd', weights, value_head_rows)
        return summed / jnp.transpose(row_total, (2, 0, 1))[..., None]
    result = lax.map(one_block, (query_head_rows, jnp.arange(PROMPT_LENGTH // block_length, dtype=jnp.int32)))
    return result.reshape(PROMPT_LENGTH, QUERY_HEADS * HEAD_SIZE)

def reference(queries, rotated_key_rows, value_row_array, residual, norm_gain, expert_ids, gate_values, w_gate_up, w_down):
    attended_rows = lax.map(attend_whole_prompt, (to_prompts(queries), to_prompts(rotated_key_rows), to_prompts(value_row_array)))
    attended_rows = from_prompts(attended_rows)
    mid_rows = (residual.astype(jnp.float32) + attended_rows).astype(jnp.bfloat16)
    mid_wide = mid_rows.astype(jnp.float32)
    inverse = lax.rsqrt(lax.optimization_barrier(jnp.mean(mid_wide * mid_wide, axis=-1, keepdims=True)) + 1e-06)
    normed = (mid_wide * inverse * norm_gain.astype(jnp.float32)).astype(jnp.bfloat16)
    token_count = N_EXP * GROUP_TOKENS
    flat_rows = normed.reshape(token_count, D)
    assign_count = token_count * TOP
    routed = expert_ids.reshape(assign_count).astype(jnp.int32)
    order = jnp.argsort(routed, stable=True).astype(jnp.int32)
    counts = jax.ops.segment_sum(jnp.ones(assign_count, jnp.int32), routed, num_segments=EXPERTS).astype(jnp.int32)
    starts = (jnp.cumsum(counts) - counts).astype(jnp.int32)
    capacity = N_CTX * N_EXP * MOST
    order = jnp.concatenate([order, jnp.zeros(capacity, jnp.int32)])
    zero_index = jnp.zeros((), jnp.int32)

    def one_expert(carried, expert):
        chosen = lax.dynamic_slice(order, (starts[expert],), (capacity,))
        live = jnp.arange(capacity, dtype=jnp.int32) < counts[expert]
        inputs = flat_rows[chosen // TOP]
        group_index = (expert // EPG).astype(jnp.int32)
        local_index = (expert % EPG).astype(jnp.int32)
        gate_up = lax.dynamic_slice(w_gate_up, (local_index * 4, group_index, zero_index, zero_index, zero_index), (4, 1, 2, QUARTER, D))[:, 0]
        down_rows = lax.dynamic_slice(w_down, (local_index * 4, group_index, zero_index, zero_index), (4, 1, QUARTER, D))[:, 0]
        summed = jnp.zeros((capacity, D), jnp.float32)
        for quarter in range(4):
            projected = lax.dot_general(gate_up[quarter], inputs, (((2,), (1,)), ((), ())), preferred_element_type=jnp.float32)
            hidden = (jax.nn.silu(projected[0]) * projected[1]).astype(jnp.bfloat16)
            part_out = lax.dot_general(hidden, down_rows[quarter], (((0,), (0,)), ((), ())), preferred_element_type=jnp.float32).astype(jnp.bfloat16)
            summed = summed + part_out.astype(jnp.float32)
        target = jnp.where(live, chosen, assign_count)
        carried = carried.at[target].set(summed.astype(jnp.bfloat16), mode='drop')
        return (carried, None)
    gathered, _ = lax.scan(one_expert, jnp.zeros((assign_count, D), jnp.bfloat16), jnp.arange(EXPERTS, dtype=jnp.int32))
    expert_out = gathered.reshape(token_count, TOP, D).astype(jnp.float32)
    gated = gate_values.reshape(token_count, TOP, 1).astype(jnp.float32) * expert_out
    layer_out = (mid_rows.reshape(token_count, D).astype(jnp.float32) + lax.optimization_barrier(jnp.sum(gated, axis=1))).astype(jnp.bfloat16)
    return layer_out.reshape(N_EXP, GROUP_TOKENS, D)
```

```python
import math

import jax
import jax.numpy as jnp
from jax import lax
from jax.experimental import pallas as pl
from jax.experimental.pallas import tpu as pltpu
from jax.sharding import Mesh
from jax.sharding import PartitionSpec as P

D = 2048
QUERY_HEADS = 16
KEY_VALUE_HEADS = 2
HEAD_SIZE = 128
TOP = 1
QUARTERS = 4

NEGATIVE_FILL = -1e30

CTX = ("z", "yh", "yl")
PROMPT = ("z", "yh")
QUARTER_AXES = ("yh", "yl")
ROUTE = ("z", "e")


def attend_kernel(pos_ref, q_ref, k_ref, v_ref, o_ref):
    rows_here = q_ref.shape[0]
    scores = lax.dot_general(
        q_ref[...], k_ref[...], (((1,), (1,)), ((), ())), preferred_element_type=jnp.float32
    ) / math.sqrt(HEAD_SIZE)
    query_pos = lax.broadcasted_iota(jnp.int32, scores.shape, 0) + pos_ref[0] * rows_here
    key_pos = lax.broadcasted_iota(jnp.int32, scores.shape, 1)
    scores = jnp.where(key_pos <= query_pos, scores, NEGATIVE_FILL)
    row_peak = jnp.max(scores, axis=1, keepdims=True)
    expo_vals = jnp.exp(scores - row_peak)
    row_total = jnp.sum(expo_vals, axis=1, keepdims=True)
    summed = jnp.dot(expo_vals.astype(jnp.bfloat16), v_ref[...], preferred_element_type=jnp.float32)
    o_ref[...] = summed / row_total


def attend(pos, queries, kv_all):
    rows_here = queries.shape[0]
    keys_all = kv_all.shape[0]
    per_kv = QUERY_HEADS // KEY_VALUE_HEADS
    flops = QUERY_HEADS * 4 * rows_here * keys_all * HEAD_SIZE
    grid_spec = pltpu.PrefetchScalarGridSpec(
        num_scalar_prefetch=1,
        grid=(QUERY_HEADS,),
        in_specs=[
            pl.BlockSpec((rows_here, HEAD_SIZE), lambda h, p: (0, h)),
            pl.BlockSpec((keys_all, HEAD_SIZE), lambda h, p: (0, h // per_kv)),
            pl.BlockSpec((keys_all, HEAD_SIZE), lambda h, p: (0, KEY_VALUE_HEADS + h // per_kv)),
        ],
        out_specs=pl.BlockSpec((rows_here, HEAD_SIZE), lambda h, p: (0, h)),
    )
    return pl.pallas_call(
        attend_kernel,
        out_shape=jax.ShapeDtypeStruct((rows_here, QUERY_HEADS * HEAD_SIZE), jnp.float32),
        grid_spec=grid_spec,
        cost_estimate=pl.CostEstimate(
            flops=flops,
            transcendentals=QUERY_HEADS * rows_here * keys_all,
            bytes_accessed=2 * kv_all.size * 2 + queries.size * 2 + rows_here * D * 4,
        ),
    )(pos, queries, kv_all, kv_all)


def on_device(
    queries,
    rotated_key_rows,
    value_row_array,
    residual,
    norm_gain,
    expert_ids,
    gate_values,
    w_gate_up,
    w_down,
):
    token_rows = queries.shape[1]
    route_count = lax.axis_size("z") * lax.axis_size("e")
    group_count = lax.axis_size("e")
    per_group = lax.axis_size("z")

    gate_up_all = lax.all_gather(w_gate_up[0, 0], QUARTER_AXES, axis=0, tiled=False)
    down_all = lax.all_gather(w_down[0, 0], QUARTER_AXES, axis=0, tiled=False)

    own_kv = jnp.concatenate([rotated_key_rows[0], value_row_array[0]], axis=-1)
    kv_all = lax.all_gather(own_kv, PROMPT, axis=0, tiled=True)
    pos = (lax.axis_index("z") * lax.axis_size("yh") + lax.axis_index("yh")).astype(jnp.int32)
    attended_rows = attend(pos.reshape(1), queries[0], kv_all)

    mid_rows = (residual[0].astype(jnp.float32) + attended_rows).astype(jnp.bfloat16)
    mid_wide = mid_rows.astype(jnp.float32)
    inverse = lax.rsqrt(jnp.mean(mid_wide * mid_wide, axis=-1, keepdims=True) + 1e-06)
    normed = (mid_wide * inverse * norm_gain).astype(jnp.bfloat16)

    slot_depth = max(2, 2 * token_rows * TOP // route_count)
    assign_count = token_rows * TOP
    routed = expert_ids[0].reshape(assign_count)
    onehot_table = (routed[:, None] == jnp.arange(route_count)[None, :]).astype(jnp.float32)
    earlier_blocks = (jnp.arange(assign_count)[:, None] > jnp.arange(assign_count)[None, :]).astype(
        jnp.float32
    )
    before = jnp.dot(
        earlier_blocks,
        onehot_table,
        precision=lax.Precision.HIGHEST,
        preferred_element_type=jnp.float32,
    )
    rank_in = jnp.sum(before * onehot_table, axis=1).astype(jnp.int32)
    slot_index = (routed % per_group * group_count + routed // per_group) * slot_depth + rank_in
    slot_count = route_count * slot_depth
    placement = (jnp.arange(slot_count)[:, None] == slot_index[None, :]).astype(jnp.bfloat16)
    normed_assign = jnp.repeat(normed, TOP, axis=0)
    outgoing = jnp.dot(placement, normed_assign, preferred_element_type=jnp.float32).astype(
        jnp.bfloat16
    )
    outgoing = outgoing.reshape(route_count, slot_depth, D)
    incoming = lax.all_to_all(outgoing, ROUTE, split_axis=0, concat_axis=0, tiled=True)
    flat_rows = incoming.reshape(slot_count, D)

    projected = jnp.einsum(
        "qguk,rk->qgur", gate_up_all, flat_rows, preferred_element_type=jnp.float32
    )
    hidden = (jax.nn.silu(projected[:, 0]) * projected[:, 1]).astype(jnp.bfloat16)
    part_out = jnp.einsum("qur,quk->qrk", hidden, down_all, preferred_element_type=jnp.float32)
    part_out = part_out.astype(jnp.bfloat16).astype(jnp.float32)
    summed = part_out[0]
    for quarter in range(1, QUARTERS):
        summed = summed + part_out[quarter]
    summed = summed.astype(jnp.bfloat16).reshape(route_count, slot_depth, D)
    delivered = lax.all_to_all(summed, ROUTE, split_axis=0, concat_axis=0, tiled=True)
    expert_out = lax.dot_general(
        placement,
        delivered.reshape(slot_count, D),
        (((0,), (0,)), ((), ())),
        preferred_element_type=jnp.float32,
    )
    gated = expert_out.reshape(token_rows, TOP, D) * gate_values[0][:, :, None]
    layer_out = (mid_wide + jnp.sum(gated, axis=1)).astype(jnp.bfloat16)
    return layer_out[None]


def solution(mesh):
    ctx_size = mesh.shape["ctx"]
    exp_size = mesh.shape["exp"]
    split_mesh = Mesh(
        mesh.devices.reshape(ctx_size // QUARTERS, QUARTERS // 2, 2, exp_size),
        ("z", "yh", "yl", "e"),
    )
    rows = P("e", CTX, None)
    return jax.shard_map(
        on_device,
        mesh=split_mesh,
        in_specs=(
            rows,
            rows,
            rows,
            rows,
            P(),
            rows,
            rows,
            P(CTX, "e", None, None, None),
            P(CTX, "e", None, None),
        ),
        out_specs=rows,
        check_vma=False,
    )
```

```python
import math

import jax
import jax.numpy as jnp
from jax import lax
from jax.experimental import pallas as pl
from jax.experimental.pallas import tpu as pltpu
from jax.sharding import Mesh
from jax.sharding import PartitionSpec as P

D = 2048
QUERY_HEADS = 16
KEY_VALUE_HEADS = 2
HEAD_SIZE = 128
TOP = 1
QUARTERS = 4

NEGATIVE_FILL = -1e30

CTX = ("z", "yh", "yl")
PROMPT = ("z", "yh")
QUARTER_AXES = ("yh", "yl")
ROUTE = ("z", "e")


def attend_kernel(pos_ref, q_ref, k_ref, v_ref, o_ref):
    rows_here = q_ref.shape[0]
    scores = lax.dot_general(
        q_ref[...], k_ref[...], (((1,), (1,)), ((), ())), preferred_element_type=jnp.float32
    ) / math.sqrt(HEAD_SIZE)
    query_pos = lax.broadcasted_iota(jnp.int32, scores.shape, 0) + pos_ref[0] * rows_here
    key_pos = lax.broadcasted_iota(jnp.int32, scores.shape, 1)
    scores = jnp.where(key_pos <= query_pos, scores, NEGATIVE_FILL)
    row_peak = jnp.max(scores, axis=1, keepdims=True)
    expo_vals = jnp.exp(scores - row_peak)
    row_total = jnp.sum(expo_vals, axis=1, keepdims=True)
    summed = jnp.dot(expo_vals.astype(jnp.bfloat16), v_ref[...], preferred_element_type=jnp.float32)
    o_ref[...] = summed / row_total


def attend(pos, queries, kv_all):
    rows_here = queries.shape[0]
    keys_all = kv_all.shape[0]
    per_kv = QUERY_HEADS // KEY_VALUE_HEADS
    flops = QUERY_HEADS * 4 * rows_here * keys_all * HEAD_SIZE
    grid_spec = pltpu.PrefetchScalarGridSpec(
        num_scalar_prefetch=1,
        grid=(QUERY_HEADS,),
        in_specs=[
            pl.BlockSpec((rows_here, HEAD_SIZE), lambda h, p: (0, h)),
            pl.BlockSpec((keys_all, HEAD_SIZE), lambda h, p: (0, h // per_kv)),
            pl.BlockSpec((keys_all, HEAD_SIZE), lambda h, p: (0, KEY_VALUE_HEADS + h // per_kv)),
        ],
        out_specs=pl.BlockSpec((rows_here, HEAD_SIZE), lambda h, p: (0, h)),
    )
    return pl.pallas_call(
        attend_kernel,
        out_shape=jax.ShapeDtypeStruct((rows_here, QUERY_HEADS * HEAD_SIZE), jnp.float32),
        grid_spec=grid_spec,
        cost_estimate=pl.CostEstimate(
            flops=flops,
            transcendentals=QUERY_HEADS * rows_here * keys_all,
            bytes_accessed=2 * kv_all.size * 2 + queries.size * 2 + rows_here * D * 4,
        ),
    )(pos, queries, kv_all, kv_all)


def on_device(
    queries,
    rotated_key_rows,
    value_row_array,
    residual,
    norm_gain,
    expert_ids,
    gate_values,
    w_gate_up,
    w_down,
):
    token_rows = queries.shape[1]
    route_count = lax.axis_size("z") * lax.axis_size("e")
    group_count = lax.axis_size("e")
    per_group = lax.axis_size("z")

    own_kv = jnp.concatenate([rotated_key_rows[0], value_row_array[0]], axis=-1)
    kv_pair = lax.all_gather(own_kv, "yh", axis=0, tiled=False)
    kv_all = lax.all_gather(kv_pair, "z", axis=0, tiled=False).reshape(-1, own_kv.shape[-1])

    own_weights = jnp.concatenate([w_gate_up[0, 0], w_down[0, 0][None]], axis=0)
    weights_all = lax.all_gather(own_weights, QUARTER_AXES, axis=0, tiled=False)
    gate_up_all = weights_all[:, :2]
    down_all = weights_all[:, 2]
    pos = (lax.axis_index("z") * lax.axis_size("yh") + lax.axis_index("yh")).astype(jnp.int32)
    attended_rows = attend(pos.reshape(1), queries[0], kv_all)

    mid_rows = (residual[0].astype(jnp.float32) + attended_rows).astype(jnp.bfloat16)
    mid_wide = mid_rows.astype(jnp.float32)
    inverse = lax.rsqrt(jnp.mean(mid_wide * mid_wide, axis=-1, keepdims=True) + 1e-06)
    normed = (mid_wide * inverse * norm_gain).astype(jnp.bfloat16)

    slot_depth = max(2, 2 * token_rows * TOP // route_count)
    assign_count = token_rows * TOP
    routed = expert_ids[0].reshape(assign_count)
    onehot_table = (routed[:, None] == jnp.arange(route_count)[None, :]).astype(jnp.float32)
    earlier_blocks = (jnp.arange(assign_count)[:, None] > jnp.arange(assign_count)[None, :]).astype(
        jnp.float32
    )
    before = jnp.dot(
        earlier_blocks,
        onehot_table,
        precision=lax.Precision.HIGHEST,
        preferred_element_type=jnp.float32,
    )
    rank_in = jnp.sum(before * onehot_table, axis=1).astype(jnp.int32)
    slot_index = (routed % per_group * group_count + routed // per_group) * slot_depth + rank_in
    slot_count = route_count * slot_depth
    placement = (jnp.arange(slot_count)[:, None] == slot_index[None, :]).astype(jnp.bfloat16)
    normed_assign = jnp.repeat(normed, TOP, axis=0)
    outgoing = jnp.dot(placement, normed_assign, preferred_element_type=jnp.float32).astype(
        jnp.bfloat16
    )
    outgoing = outgoing.reshape(route_count, slot_depth, D)
    incoming = lax.all_to_all(outgoing, ROUTE, split_axis=0, concat_axis=0, tiled=True)
    flat_rows = incoming.reshape(slot_count, D)

    projected = jnp.einsum(
        "qguk,rk->qgur", gate_up_all, flat_rows, preferred_element_type=jnp.float32
    )
    hidden = (jax.nn.silu(projected[:, 0]) * projected[:, 1]).astype(jnp.bfloat16)
    part_out = jnp.einsum("qur,quk->qrk", hidden, down_all, preferred_element_type=jnp.float32)
    part_out = part_out.astype(jnp.bfloat16).astype(jnp.float32)
    summed = part_out[0]
    for quarter in range(1, QUARTERS):
        summed = summed + part_out[quarter]
    summed = summed.astype(jnp.bfloat16).reshape(route_count, slot_depth, D)
    delivered = lax.all_to_all(summed, ROUTE, split_axis=0, concat_axis=0, tiled=True)
    expert_out = lax.dot_general(
        placement,
        delivered.reshape(slot_count, D),
        (((0,), (0,)), ((), ())),
        preferred_element_type=jnp.float32,
    )
    gated = expert_out.reshape(token_rows, TOP, D) * gate_values[0][:, :, None]
    layer_out = (mid_wide + jnp.sum(gated, axis=1)).astype(jnp.bfloat16)
    return layer_out[None]


def solution(mesh):
    ctx_size = mesh.shape["ctx"]
    exp_size = mesh.shape["exp"]
    split_mesh = Mesh(
        mesh.devices.reshape(ctx_size // QUARTERS, QUARTERS // 2, 2, exp_size),
        ("z", "yh", "yl", "e"),
    )
    rows = P("e", CTX, None)
    return jax.shard_map(
        on_device,
        mesh=split_mesh,
        in_specs=(
            rows,
            rows,
            rows,
            rows,
            P(),
            rows,
            rows,
            P(CTX, "e", None, None, None),
            P(CTX, "e", None, None),
        ),
        out_specs=rows,
        check_vma=False,
    )
```

```python
import math

import jax
import jax.numpy as jnp
from jax import lax
from jax.experimental import pallas as pl
from jax.experimental.pallas import tpu as pltpu
from jax.sharding import Mesh
from jax.sharding import PartitionSpec as P

D = 2048
QUERY_HEADS = 16
KEY_VALUE_HEADS = 2
HEAD_SIZE = 128
TOP = 1
QUARTERS = 4

NEGATIVE_FILL = -1e30

CTX = ("z", "yh", "yl")
QUARTER_AXES = ("yh", "yl")
ROUTE = ("z", "e")


def attend_kernel(pos_ref, q_ref, k_ref, v_ref, o_ref, bias_ref):
    rows_here = q_ref.shape[0]

    @pl.when(pl.program_id(0) == 0)
    def _():
        query_pos = lax.broadcasted_iota(jnp.int32, bias_ref.shape, 0) + pos_ref[0] * rows_here
        key_pos = lax.broadcasted_iota(jnp.int32, bias_ref.shape, 1)
        bias_ref[...] = jnp.where(key_pos <= query_pos, 0.0, NEGATIVE_FILL).astype(jnp.float32)

    scores = lax.dot_general(
        q_ref[...], k_ref[...], (((1,), (1,)), ((), ())), preferred_element_type=jnp.float32
    ) + bias_ref[...]
    row_peak = jnp.max(scores, axis=1, keepdims=True)
    expo_vals = jnp.exp((scores - row_peak) * (1.0 / math.sqrt(HEAD_SIZE)))
    row_total = jnp.sum(expo_vals, axis=1, keepdims=True)
    summed = jnp.dot(expo_vals.astype(jnp.bfloat16), v_ref[...], preferred_element_type=jnp.float32)
    o_ref[...] = summed / row_total


def attend(pos, queries, kv_all):
    rows_here = queries.shape[0]
    keys_all = kv_all.shape[0]
    per_kv = QUERY_HEADS // KEY_VALUE_HEADS
    flops = QUERY_HEADS * 4 * rows_here * keys_all * HEAD_SIZE
    grid_spec = pltpu.PrefetchScalarGridSpec(
        num_scalar_prefetch=1,
        grid=(QUERY_HEADS,),
        in_specs=[
            pl.BlockSpec((rows_here, HEAD_SIZE), lambda h, p: (0, h)),
            pl.BlockSpec((keys_all, HEAD_SIZE), lambda h, p: (0, h // per_kv)),
            pl.BlockSpec((keys_all, HEAD_SIZE), lambda h, p: (0, KEY_VALUE_HEADS + h // per_kv)),
        ],
        out_specs=pl.BlockSpec((rows_here, HEAD_SIZE), lambda h, p: (0, h)),
        scratch_shapes=[pltpu.VMEM((rows_here, keys_all), jnp.float32)],
    )
    return pl.pallas_call(
        attend_kernel,
        out_shape=jax.ShapeDtypeStruct((rows_here, QUERY_HEADS * HEAD_SIZE), jnp.float32),
        grid_spec=grid_spec,
        cost_estimate=pl.CostEstimate(
            flops=flops,
            transcendentals=QUERY_HEADS * rows_here * keys_all,
            bytes_accessed=2 * kv_all.size * 2 + queries.size * 2 + rows_here * D * 4,
        ),
    )(pos, queries, kv_all, kv_all)


def layer(
    queries,
    rotated_key_rows,
    value_row_array,
    residual,
    norm_gain,
    expert_ids,
    gate_values,
    w_gate_up,
    w_down,
):
    token_rows = queries.shape[1]
    route_count = lax.axis_size("z") * lax.axis_size("e")
    group_count = lax.axis_size("e")
    per_group = lax.axis_size("z")

    own_kv = jnp.concatenate([rotated_key_rows[0], value_row_array[0]], axis=-1)
    kv_pair = lax.all_gather(own_kv, "yh", axis=0, tiled=False)
    kv_all = lax.all_gather(kv_pair, "z", axis=0, tiled=False).reshape(-1, own_kv.shape[-1])

    quarter_count = lax.axis_size(QUARTER_AXES)
    own_weights = jnp.concatenate([w_gate_up[0, 0], w_down[0, 0][None]], axis=0)
    quarter_weights = [own_weights]
    for shift in range(1, quarter_count):
        pairs = [(q, (q + shift) % quarter_count) for q in range(quarter_count)]
        quarter_weights.append(lax.ppermute(own_weights, QUARTER_AXES, pairs))
    pos = (lax.axis_index("z") * lax.axis_size("yh") + lax.axis_index("yh")).astype(jnp.int32)
    attended_rows = attend(pos.reshape(1), queries[0], kv_all)

    mid_rows = (residual[0].astype(jnp.float32) + attended_rows).astype(jnp.bfloat16)
    mid_wide = mid_rows.astype(jnp.float32)
    inverse = lax.rsqrt(jnp.mean(mid_wide * mid_wide, axis=-1, keepdims=True) + 1e-06)
    normed = (mid_wide * inverse * norm_gain).astype(jnp.bfloat16)

    slot_depth = max(2, 2 * token_rows * TOP // route_count)
    assign_count = token_rows * TOP
    routed = expert_ids[0].reshape(assign_count)
    onehot_table = (routed[:, None] == jnp.arange(route_count)[None, :]).astype(jnp.float32)
    earlier_blocks = (jnp.arange(assign_count)[:, None] > jnp.arange(assign_count)[None, :]).astype(
        jnp.float32
    )
    before = jnp.dot(
        earlier_blocks,
        onehot_table,
        precision=lax.Precision.HIGHEST,
        preferred_element_type=jnp.float32,
    )
    rank_in = jnp.sum(before * onehot_table, axis=1).astype(jnp.int32)
    slot_index = (routed % per_group * group_count + routed // per_group) * slot_depth + rank_in
    slot_count = route_count * slot_depth
    placement = (jnp.arange(slot_count)[:, None] == slot_index[None, :]).astype(jnp.bfloat16)
    normed_assign = jnp.repeat(normed, TOP, axis=0)
    outgoing = jnp.dot(placement, normed_assign, preferred_element_type=jnp.float32).astype(
        jnp.bfloat16
    )
    outgoing = outgoing.reshape(route_count, slot_depth, D)
    incoming = lax.all_to_all(outgoing, ROUTE, split_axis=0, concat_axis=0, tiled=True)
    flat_rows = incoming.reshape(slot_count, D)

    summed = None
    for weights in quarter_weights:
        gate_up, down_rows = weights[:2], weights[2]
        projected = lax.dot_general(
            gate_up, flat_rows, (((2,), (1,)), ((), ())), preferred_element_type=jnp.float32
        )
        hidden = (jax.nn.silu(projected[0]) * projected[1]).astype(jnp.bfloat16)
        part_out = lax.dot_general(
            hidden, down_rows, (((0,), (0,)), ((), ())), preferred_element_type=jnp.float32
        )
        part_out = part_out.astype(jnp.bfloat16).astype(jnp.float32)
        summed = part_out if summed is None else summed + part_out
    summed = summed.astype(jnp.bfloat16).reshape(route_count, slot_depth, D)
    delivered = lax.all_to_all(summed, ROUTE, split_axis=0, concat_axis=0, tiled=True)
    expert_out = lax.dot_general(
        placement,
        delivered.reshape(slot_count, D),
        (((0,), (0,)), ((), ())),
        preferred_element_type=jnp.float32,
    )
    gated = expert_out.reshape(token_rows, TOP, D) * gate_values[0][:, :, None]
    layer_out = (mid_wide + jnp.sum(gated, axis=1)).astype(jnp.bfloat16)
    return layer_out[None]


def solution(mesh):
    ctx_size = mesh.shape["ctx"]
    exp_size = mesh.shape["exp"]
    split_mesh = Mesh(
        mesh.devices.reshape(ctx_size // QUARTERS, QUARTERS // 2, 2, exp_size),
        ("z", "yh", "yl", "e"),
    )
    rows = P("e", CTX, None)
    return jax.shard_map(
        layer,
        mesh=split_mesh,
        in_specs=(
            rows,
            rows,
            rows,
            rows,
            P(),
            rows,
            rows,
            P(CTX, "e", None, None, None),
            P(CTX, "e", None, None),
        ),
        out_specs=rows,
        check_vma=False,
    )
```

```python
import math

import jax
import jax.numpy as jnp
from jax import lax
from jax.experimental import pallas as pl
from jax.experimental.pallas import tpu as pltpu
from jax.sharding import Mesh
from jax.sharding import PartitionSpec as P

D = 2048
QUERY_HEADS = 16
KEY_VALUE_HEADS = 2
HEAD_SIZE = 128
TOP = 1
QUARTERS = 4

NEGATIVE_FILL = -1e30

CTX = ("z", "yh", "yl")
QUARTER_AXES = ("yh", "yl")
ROUTE = ("z", "e")


def attend_kernel(pos_ref, q_ref, k_ref, v_ref, o_ref, bias_ref):
    rows_here = q_ref.shape[0]

    @pl.when(pl.program_id(0) == 0)
    def _():
        query_pos = lax.broadcasted_iota(jnp.int32, bias_ref.shape, 0) + pos_ref[0] * rows_here
        key_pos = lax.broadcasted_iota(jnp.int32, bias_ref.shape, 1)
        bias_ref[...] = jnp.where(key_pos <= query_pos, 0.0, NEGATIVE_FILL).astype(jnp.float32)

    scores = lax.dot_general(
        q_ref[...], k_ref[...], (((1,), (1,)), ((), ())), preferred_element_type=jnp.float32
    ) + bias_ref[...]
    row_peak = jnp.max(scores, axis=1, keepdims=True)
    expo_vals = jnp.exp((scores - row_peak) * (1.0 / math.sqrt(HEAD_SIZE)))
    row_total = jnp.sum(expo_vals, axis=1, keepdims=True)
    summed = jnp.dot(expo_vals.astype(jnp.bfloat16), v_ref[...], preferred_element_type=jnp.float32)
    o_ref[...] = summed / row_total


def attend(pos, queries, kv_all):
    rows_here = queries.shape[0]
    keys_all = kv_all.shape[0]
    per_kv = QUERY_HEADS // KEY_VALUE_HEADS
    flops = QUERY_HEADS * 4 * rows_here * keys_all * HEAD_SIZE
    grid_spec = pltpu.PrefetchScalarGridSpec(
        num_scalar_prefetch=1,
        grid=(QUERY_HEADS,),
        in_specs=[
            pl.BlockSpec((rows_here, HEAD_SIZE), lambda h, p: (0, h)),
            pl.BlockSpec((keys_all, HEAD_SIZE), lambda h, p: (0, h // per_kv)),
            pl.BlockSpec((keys_all, HEAD_SIZE), lambda h, p: (0, KEY_VALUE_HEADS + h // per_kv)),
        ],
        out_specs=pl.BlockSpec((rows_here, HEAD_SIZE), lambda h, p: (0, h)),
        scratch_shapes=[pltpu.VMEM((rows_here, keys_all), jnp.float32)],
    )
    return pl.pallas_call(
        attend_kernel,
        out_shape=jax.ShapeDtypeStruct((rows_here, QUERY_HEADS * HEAD_SIZE), jnp.float32),
        grid_spec=grid_spec,
        cost_estimate=pl.CostEstimate(
            flops=flops,
            transcendentals=QUERY_HEADS * rows_here * keys_all,
            bytes_accessed=2 * kv_all.size * 2 + queries.size * 2 + rows_here * D * 4,
        ),
    )(pos, queries, kv_all, kv_all)


def expert_kernel(rows_ref, w0_ref, w1_ref, w2_ref, w3_ref, o_ref, wbuf, sems):
    hid = w0_ref.shape[1]
    sources = (w0_ref, w1_ref, w2_ref, w3_ref)
    copies = [
        pltpu.make_async_copy(src, wbuf.at[i], sems.at[i]) for i, src in enumerate(sources)
    ]
    for copy in copies:
        copy.start()
    rows = rows_ref[...]
    total = None
    for i, copy in enumerate(copies):
        copy.wait()
        gate_up = wbuf[i, 0:2].reshape(2 * hid, rows.shape[1])
        projected = lax.dot_general(
            gate_up, rows, (((1,), (1,)), ((), ())), preferred_element_type=jnp.float32
        )
        gate, up = projected[:hid], projected[hid:]
        hidden = (gate / (1.0 + jnp.exp(-gate)) * up).astype(jnp.bfloat16)
        part_out = lax.dot_general(
            hidden, wbuf[i, 2], (((0,), (0,)), ((), ())), preferred_element_type=jnp.float32
        )
        part_out = part_out.astype(jnp.bfloat16).astype(jnp.float32)
        total = part_out if total is None else total + part_out
    o_ref[...] = total.astype(o_ref.dtype)


def experts(rows, quarter_weights):
    count, hid, width = quarter_weights[0].shape
    slots = rows.shape[0]
    return pl.pallas_call(
        expert_kernel,
        out_shape=jax.ShapeDtypeStruct((slots, width), jnp.bfloat16),
        in_specs=[pl.BlockSpec(memory_space=pltpu.VMEM)]
        + [pl.BlockSpec(memory_space=pl.ANY)] * len(quarter_weights),
        out_specs=pl.BlockSpec(memory_space=pltpu.VMEM),
        scratch_shapes=[
            pltpu.VMEM((len(quarter_weights), count, hid, width), jnp.bfloat16),
            pltpu.SemaphoreType.DMA((len(quarter_weights),)),
        ],
        compiler_params=pltpu.CompilerParams(vmem_limit_bytes=48 * 1024 * 1024),
        cost_estimate=pl.CostEstimate(
            flops=2 * slots * count * hid * width * len(quarter_weights),
            transcendentals=slots * hid * len(quarter_weights),
            bytes_accessed=2 * (count * hid * width * len(quarter_weights) + 2 * slots * width),
        ),
    )(rows, *quarter_weights)


def layer(
    queries,
    rotated_key_rows,
    value_row_array,
    residual,
    norm_gain,
    expert_ids,
    gate_values,
    w_gate_up,
    w_down,
):
    token_rows = queries.shape[1]
    route_count = lax.axis_size("z") * lax.axis_size("e")
    group_count = lax.axis_size("e")
    per_group = lax.axis_size("z")

    own_kv = jnp.concatenate([rotated_key_rows[0], value_row_array[0]], axis=-1)
    kv_pair = lax.all_gather(own_kv, "yh", axis=0, tiled=False)
    kv_all = lax.all_gather(kv_pair, "z", axis=0, tiled=False).reshape(-1, own_kv.shape[-1])

    quarter_count = lax.axis_size(QUARTER_AXES)
    own_weights = jnp.concatenate([w_gate_up[0, 0], w_down[0, 0][None]], axis=0)
    quarter_weights = [own_weights]
    for shift in range(1, quarter_count):
        pairs = [(q, (q + shift) % quarter_count) for q in range(quarter_count)]
        quarter_weights.append(lax.ppermute(own_weights, QUARTER_AXES, pairs))
    pos = (lax.axis_index("z") * lax.axis_size("yh") + lax.axis_index("yh")).astype(jnp.int32)
    attended_rows = attend(pos.reshape(1), queries[0], kv_all)

    mid_rows = (residual[0].astype(jnp.float32) + attended_rows).astype(jnp.bfloat16)
    mid_wide = mid_rows.astype(jnp.float32)
    inverse = lax.rsqrt(jnp.mean(mid_wide * mid_wide, axis=-1, keepdims=True) + 1e-06)
    normed = (mid_wide * inverse * norm_gain).astype(jnp.bfloat16)

    slot_depth = max(2, 2 * token_rows * TOP // route_count)
    assign_count = token_rows * TOP
    routed = expert_ids[0].reshape(assign_count)
    onehot_table = (routed[:, None] == jnp.arange(route_count)[None, :]).astype(jnp.float32)
    earlier_blocks = (jnp.arange(assign_count)[:, None] > jnp.arange(assign_count)[None, :]).astype(
        jnp.float32
    )
    before = jnp.dot(
        earlier_blocks,
        onehot_table,
        precision=lax.Precision.HIGHEST,
        preferred_element_type=jnp.float32,
    )
    rank_in = jnp.sum(before * onehot_table, axis=1).astype(jnp.int32)
    slot_index = (routed % per_group * group_count + routed // per_group) * slot_depth + rank_in
    slot_count = route_count * slot_depth
    placement = (jnp.arange(slot_count)[:, None] == slot_index[None, :]).astype(jnp.bfloat16)
    normed_assign = jnp.repeat(normed, TOP, axis=0)
    outgoing = jnp.dot(placement, normed_assign, preferred_element_type=jnp.float32).astype(
        jnp.bfloat16
    )
    outgoing = outgoing.reshape(route_count, slot_depth, D)
    incoming = lax.all_to_all(outgoing, ROUTE, split_axis=0, concat_axis=0, tiled=True)
    flat_rows = incoming.reshape(slot_count, D)

    summed = experts(flat_rows, quarter_weights)
    summed = summed.reshape(route_count, slot_depth, D)
    delivered = lax.all_to_all(summed, ROUTE, split_axis=0, concat_axis=0, tiled=True)
    expert_out = lax.dot_general(
        placement,
        delivered.reshape(slot_count, D),
        (((0,), (0,)), ((), ())),
        preferred_element_type=jnp.float32,
    )
    gated = expert_out.reshape(token_rows, TOP, D) * gate_values[0][:, :, None]
    layer_out = (mid_wide + jnp.sum(gated, axis=1)).astype(jnp.bfloat16)
    return layer_out[None]


def solution(mesh):
    ctx_size = mesh.shape["ctx"]
    exp_size = mesh.shape["exp"]
    split_mesh = Mesh(
        mesh.devices.reshape(ctx_size // QUARTERS, QUARTERS // 2, 2, exp_size),
        ("z", "yh", "yl", "e"),
    )
    rows = P("e", CTX, None)
    return jax.shard_map(
        layer,
        mesh=split_mesh,
        in_specs=(
            rows,
            rows,
            rows,
            rows,
            P(),
            rows,
            rows,
            P(CTX, "e", None, None, None),
            P(CTX, "e", None, None),
        ),
        out_specs=rows,
        check_vma=False,
    )
```

```python
import math

import jax
import jax.numpy as jnp
from jax import lax
from jax.experimental import pallas as pl
from jax.experimental.pallas import tpu as pltpu
from jax.sharding import Mesh
from jax.sharding import PartitionSpec as P

D = 2048
QUERY_HEADS = 16
KEY_VALUE_HEADS = 2
HEAD_SIZE = 128
TOP = 1
QUARTERS = 4

NEGATIVE_FILL = -1e30

CTX = ("z", "yh", "yl")
QUARTER_AXES = ("yh", "yl")
ROUTE = ("z", "e")


def attend_kernel(pos_ref, q_ref, k_ref, v_ref, o_ref, bias_ref):
    rows_here = q_ref.shape[0]

    @pl.when(pl.program_id(0) == 0)
    def _():
        query_pos = lax.broadcasted_iota(jnp.int32, bias_ref.shape, 0) + pos_ref[0] * rows_here
        key_pos = lax.broadcasted_iota(jnp.int32, bias_ref.shape, 1)
        bias_ref[...] = jnp.where(key_pos <= query_pos, 0.0, NEGATIVE_FILL).astype(jnp.float32)

    scores = lax.dot_general(
        q_ref[...], k_ref[...], (((1,), (1,)), ((), ())), preferred_element_type=jnp.float32
    ) + bias_ref[...]
    row_peak = jnp.max(scores, axis=1, keepdims=True)
    expo_vals = jnp.exp((scores - row_peak) * (1.0 / math.sqrt(HEAD_SIZE)))
    row_total = jnp.sum(expo_vals, axis=1, keepdims=True)
    summed = jnp.dot(expo_vals.astype(jnp.bfloat16), v_ref[...], preferred_element_type=jnp.float32)
    o_ref[...] = summed / row_total


def attend(pos, queries, kv_all):
    rows_here = queries.shape[0]
    keys_all = kv_all.shape[0]
    per_kv = QUERY_HEADS // KEY_VALUE_HEADS
    flops = QUERY_HEADS * 4 * rows_here * keys_all * HEAD_SIZE
    grid_spec = pltpu.PrefetchScalarGridSpec(
        num_scalar_prefetch=1,
        grid=(QUERY_HEADS,),
        in_specs=[
            pl.BlockSpec((rows_here, HEAD_SIZE), lambda h, p: (0, h)),
            pl.BlockSpec((keys_all, HEAD_SIZE), lambda h, p: (0, h // per_kv)),
            pl.BlockSpec((keys_all, HEAD_SIZE), lambda h, p: (0, KEY_VALUE_HEADS + h // per_kv)),
        ],
        out_specs=pl.BlockSpec((rows_here, HEAD_SIZE), lambda h, p: (0, h)),
        scratch_shapes=[pltpu.VMEM((rows_here, keys_all), jnp.float32)],
    )
    return pl.pallas_call(
        attend_kernel,
        out_shape=jax.ShapeDtypeStruct((rows_here, QUERY_HEADS * HEAD_SIZE), jnp.float32),
        grid_spec=grid_spec,
        cost_estimate=pl.CostEstimate(
            flops=flops,
            transcendentals=QUERY_HEADS * rows_here * keys_all,
            bytes_accessed=2 * kv_all.size * 2 + queries.size * 2 + rows_here * D * 4,
        ),
    )(pos, queries, kv_all, kv_all)


def expert_kernel(rows_ref, w0_ref, w1_ref, w2_ref, w3_ref, o_ref, wbuf, sems):
    hid = w0_ref.shape[1]
    sources = (w0_ref, w1_ref, w2_ref, w3_ref)
    copies = [
        pltpu.make_async_copy(src, wbuf.at[i], sems.at[i]) for i, src in enumerate(sources)
    ]
    for copy in copies:
        copy.start()
    depth = rows_ref.shape[1]
    planes = [rows_ref[:, s, :] for s in range(depth)]
    totals = [None] * depth
    for i, copy in enumerate(copies):
        copy.wait()
        gate_up = wbuf[i, 0:2].reshape(2 * hid, rows_ref.shape[2])
        for s, rows in enumerate(planes):
            projected = lax.dot_general(
                gate_up, rows, (((1,), (1,)), ((), ())), preferred_element_type=jnp.float32
            )
            gate, up = projected[:hid], projected[hid:]
            hidden = (gate / (1.0 + jnp.exp(-gate)) * up).astype(jnp.bfloat16)
            part_out = lax.dot_general(
                hidden, wbuf[i, 2], (((0,), (0,)), ((), ())), preferred_element_type=jnp.float32
            )
            part_out = part_out.astype(jnp.bfloat16).astype(jnp.float32)
            totals[s] = part_out if totals[s] is None else totals[s] + part_out
    for s in range(depth):
        o_ref[:, s, :] = totals[s].astype(o_ref.dtype)


def experts(rows, quarter_weights):
    count, hid, width = quarter_weights[0].shape
    slots = rows.shape[0] * rows.shape[1]
    return pl.pallas_call(
        expert_kernel,
        out_shape=jax.ShapeDtypeStruct(rows.shape, jnp.bfloat16),
        in_specs=[pl.BlockSpec(memory_space=pltpu.VMEM)]
        + [pl.BlockSpec(memory_space=pl.ANY)] * len(quarter_weights),
        out_specs=pl.BlockSpec(memory_space=pltpu.VMEM),
        scratch_shapes=[
            pltpu.VMEM((len(quarter_weights), count, hid, width), jnp.bfloat16),
            pltpu.SemaphoreType.DMA((len(quarter_weights),)),
        ],
        compiler_params=pltpu.CompilerParams(vmem_limit_bytes=48 * 1024 * 1024),
        cost_estimate=pl.CostEstimate(
            flops=2 * slots * count * hid * width * len(quarter_weights),
            transcendentals=slots * hid * len(quarter_weights),
            bytes_accessed=2 * (count * hid * width * len(quarter_weights) + 2 * slots * width),
        ),
    )(rows, *quarter_weights)


def layer(
    queries,
    rotated_key_rows,
    value_row_array,
    residual,
    norm_gain,
    expert_ids,
    gate_values,
    w_gate_up,
    w_down,
):
    token_rows = queries.shape[1]
    route_count = lax.axis_size("z") * lax.axis_size("e")
    group_count = lax.axis_size("e")
    per_group = lax.axis_size("z")

    own_kv = jnp.concatenate([rotated_key_rows[0], value_row_array[0]], axis=-1)
    kv_pair = lax.all_gather(own_kv, "yh", axis=0, tiled=False)
    kv_all = lax.all_gather(kv_pair, "z", axis=0, tiled=False).reshape(-1, own_kv.shape[-1])

    quarter_count = lax.axis_size(QUARTER_AXES)
    own_weights = jnp.concatenate([w_gate_up[0, 0], w_down[0, 0][None]], axis=0)
    quarter_weights = [own_weights]
    for shift in range(1, quarter_count):
        pairs = [(q, (q + shift) % quarter_count) for q in range(quarter_count)]
        quarter_weights.append(lax.ppermute(own_weights, QUARTER_AXES, pairs))
    pos = (lax.axis_index("z") * lax.axis_size("yh") + lax.axis_index("yh")).astype(jnp.int32)
    attended_rows = attend(pos.reshape(1), queries[0], kv_all)

    mid_rows = (residual[0].astype(jnp.float32) + attended_rows).astype(jnp.bfloat16)
    mid_wide = mid_rows.astype(jnp.float32)
    inverse = lax.rsqrt(jnp.mean(mid_wide * mid_wide, axis=-1, keepdims=True) + 1e-06)
    normed = (mid_wide * inverse * norm_gain).astype(jnp.bfloat16)

    slot_depth = max(2, 2 * token_rows * TOP // route_count)
    assign_count = token_rows * TOP
    routed = expert_ids[0].reshape(assign_count)
    onehot_table = (routed[:, None] == jnp.arange(route_count)[None, :]).astype(jnp.float32)
    earlier_blocks = (jnp.arange(assign_count)[:, None] > jnp.arange(assign_count)[None, :]).astype(
        jnp.float32
    )
    before = jnp.dot(
        earlier_blocks,
        onehot_table,
        precision=lax.Precision.HIGHEST,
        preferred_element_type=jnp.float32,
    )
    rank_in = jnp.sum(before * onehot_table, axis=1).astype(jnp.int32)
    slot_index = (routed % per_group * group_count + routed // per_group) * slot_depth + rank_in
    slot_count = route_count * slot_depth
    placement = (jnp.arange(slot_count)[:, None] == slot_index[None, :]).astype(jnp.bfloat16)
    normed_assign = jnp.repeat(normed, TOP, axis=0)
    placement_3d = placement.reshape(route_count, slot_depth, assign_count)
    outgoing = jnp.einsum(
        "dst,tk->dsk", placement_3d, normed_assign, preferred_element_type=jnp.float32
    ).astype(jnp.bfloat16)
    incoming = lax.all_to_all(outgoing, ROUTE, split_axis=0, concat_axis=0, tiled=True)

    summed = experts(incoming, quarter_weights)
    delivered = lax.all_to_all(summed, ROUTE, split_axis=0, concat_axis=0, tiled=True)
    expert_out = jnp.einsum(
        "dst,dsk->tk", placement_3d, delivered, preferred_element_type=jnp.float32
    )
    gated = expert_out.reshape(token_rows, TOP, D) * gate_values[0][:, :, None]
    layer_out = (mid_wide + jnp.sum(gated, axis=1)).astype(jnp.bfloat16)
    return layer_out[None]


def solution(mesh):
    ctx_size = mesh.shape["ctx"]
    exp_size = mesh.shape["exp"]
    split_mesh = Mesh(
        mesh.devices.reshape(ctx_size // QUARTERS, QUARTERS // 2, 2, exp_size),
        ("z", "yh", "yl", "e"),
    )
    rows = P("e", CTX, None)
    return jax.shard_map(
        layer,
        mesh=split_mesh,
        in_specs=(
            rows,
            rows,
            rows,
            rows,
            P(),
            rows,
            rows,
            P(CTX, "e", None, None, None),
            P(CTX, "e", None, None),
        ),
        out_specs=rows,
        check_vma=False,
    )
```

```python
import math

import jax
import jax.numpy as jnp
from jax import lax
from jax.experimental import pallas as pl
from jax.experimental.pallas import tpu as pltpu
from jax.sharding import Mesh
from jax.sharding import PartitionSpec as P

D = 2048
QUERY_HEADS = 16
KEY_VALUE_HEADS = 2
HEAD_SIZE = 128
TOP = 1
QUARTERS = 4

NEGATIVE_FILL = -1e30

CTX = ("z", "yh", "yl")
QUARTER_AXES = ("yh", "yl")
ROUTE = ("z", "e")


def attend_kernel(pos_ref, q_ref, k_ref, v_ref, o_ref):
    rows_here = q_ref.shape[0]
    scores = lax.dot_general(
        q_ref[...], k_ref[...], (((1,), (1,)), ((), ())), preferred_element_type=jnp.float32
    ) / math.sqrt(HEAD_SIZE)
    query_pos = lax.broadcasted_iota(jnp.int32, scores.shape, 0) + pos_ref[0] * rows_here
    key_pos = lax.broadcasted_iota(jnp.int32, scores.shape, 1)
    scores = jnp.where(key_pos <= query_pos, scores, NEGATIVE_FILL)
    row_peak = jnp.max(scores, axis=1, keepdims=True)
    expo_vals = jnp.exp(scores - row_peak)
    row_total = jnp.sum(expo_vals, axis=1, keepdims=True)
    summed = jnp.dot(expo_vals.astype(jnp.bfloat16), v_ref[...], preferred_element_type=jnp.float32)
    o_ref[...] = summed / row_total


def attend(pos, queries, kv_all):
    rows_here = queries.shape[0]
    keys_all = kv_all.shape[0]
    per_kv = QUERY_HEADS // KEY_VALUE_HEADS
    flops = QUERY_HEADS * 4 * rows_here * keys_all * HEAD_SIZE
    grid_spec = pltpu.PrefetchScalarGridSpec(
        num_scalar_prefetch=1,
        grid=(QUERY_HEADS,),
        in_specs=[
            pl.BlockSpec((rows_here, HEAD_SIZE), lambda h, p: (0, h)),
            pl.BlockSpec((keys_all, HEAD_SIZE), lambda h, p: (0, h // per_kv)),
            pl.BlockSpec((keys_all, HEAD_SIZE), lambda h, p: (0, KEY_VALUE_HEADS + h // per_kv)),
        ],
        out_specs=pl.BlockSpec((rows_here, HEAD_SIZE), lambda h, p: (0, h)),
    )
    return pl.pallas_call(
        attend_kernel,
        out_shape=jax.ShapeDtypeStruct((rows_here, QUERY_HEADS * HEAD_SIZE), jnp.float32),
        grid_spec=grid_spec,
        cost_estimate=pl.CostEstimate(
            flops=flops,
            transcendentals=QUERY_HEADS * rows_here * keys_all,
            bytes_accessed=2 * kv_all.size * 2 + queries.size * 2 + rows_here * D * 4,
        ),
    )(pos, queries, kv_all, kv_all)


def expert_kernel(rows_ref, w0_ref, w1_ref, w2_ref, w3_ref, o_ref, wbuf, sems):
    hid = w0_ref.shape[1]
    sources = (w0_ref, w1_ref, w2_ref, w3_ref)
    copies = [
        pltpu.make_async_copy(src, wbuf.at[i], sems.at[i]) for i, src in enumerate(sources)
    ]
    for copy in copies:
        copy.start()
    rows = rows_ref[...]
    total = None
    for i, copy in enumerate(copies):
        copy.wait()
        gate_up = wbuf[i, 0:2].reshape(2 * hid, rows.shape[1])
        projected = lax.dot_general(
            gate_up, rows, (((1,), (1,)), ((), ())), preferred_element_type=jnp.float32
        )
        gate, up = projected[:hid], projected[hid:]
        hidden = (gate / (1.0 + jnp.exp(-gate)) * up).astype(jnp.bfloat16)
        part_out = lax.dot_general(
            hidden, wbuf[i, 2], (((0,), (0,)), ((), ())), preferred_element_type=jnp.float32
        )
        part_out = part_out.astype(jnp.bfloat16).astype(jnp.float32)
        total = part_out if total is None else total + part_out
    o_ref[...] = total.astype(o_ref.dtype)


def experts(rows, quarter_weights):
    count, hid, width = quarter_weights[0].shape
    slots = rows.shape[0]
    return pl.pallas_call(
        expert_kernel,
        out_shape=jax.ShapeDtypeStruct((slots, width), jnp.bfloat16),
        in_specs=[pl.BlockSpec(memory_space=pltpu.VMEM)]
        + [pl.BlockSpec(memory_space=pl.ANY)] * len(quarter_weights),
        out_specs=pl.BlockSpec(memory_space=pltpu.VMEM),
        scratch_shapes=[
            pltpu.VMEM((len(quarter_weights), count, hid, width), jnp.bfloat16),
            pltpu.SemaphoreType.DMA((len(quarter_weights),)),
        ],
        compiler_params=pltpu.CompilerParams(vmem_limit_bytes=48 * 1024 * 1024),
        cost_estimate=pl.CostEstimate(
            flops=2 * slots * count * hid * width * len(quarter_weights),
            transcendentals=slots * hid * len(quarter_weights),
            bytes_accessed=2 * (count * hid * width * len(quarter_weights) + 2 * slots * width),
        ),
    )(rows, *quarter_weights)


def layer(
    queries,
    rotated_key_rows,
    value_row_array,
    residual,
    norm_gain,
    expert_ids,
    gate_values,
    w_gate_up,
    w_down,
):
    token_rows = queries.shape[1]
    route_count = lax.axis_size("z") * lax.axis_size("e")
    group_count = lax.axis_size("e")
    per_group = lax.axis_size("z")

    own_kv = jnp.concatenate([rotated_key_rows[0], value_row_array[0]], axis=-1)
    kv_pair = lax.all_gather(own_kv, "yh", axis=0, tiled=False)
    kv_all = lax.all_gather(kv_pair, "z", axis=0, tiled=False).reshape(-1, own_kv.shape[-1])

    quarter_count = lax.axis_size(QUARTER_AXES)
    own_weights = jnp.concatenate([w_gate_up[0, 0], w_down[0, 0][None]], axis=0)
    quarter_weights = [own_weights]
    for shift in range(1, quarter_count):
        pairs = [(q, (q + shift) % quarter_count) for q in range(quarter_count)]
        quarter_weights.append(lax.ppermute(own_weights, QUARTER_AXES, pairs))
    pos = (lax.axis_index("z") * lax.axis_size("yh") + lax.axis_index("yh")).astype(jnp.int32)
    attended_rows = attend(pos.reshape(1), queries[0], kv_all)

    mid_rows = (residual[0].astype(jnp.float32) + attended_rows).astype(jnp.bfloat16)
    mid_wide = mid_rows.astype(jnp.float32)
    inverse = lax.rsqrt(jnp.mean(mid_wide * mid_wide, axis=-1, keepdims=True) + 1e-06)
    normed = (mid_wide * inverse * norm_gain).astype(jnp.bfloat16)

    slot_depth = max(2, 2 * token_rows * TOP // route_count)
    assign_count = token_rows * TOP
    routed = expert_ids[0].reshape(assign_count)
    onehot_table = (routed[:, None] == jnp.arange(route_count)[None, :]).astype(jnp.float32)
    earlier_blocks = (jnp.arange(assign_count)[:, None] > jnp.arange(assign_count)[None, :]).astype(
        jnp.float32
    )
    before = jnp.dot(
        earlier_blocks,
        onehot_table,
        precision=lax.Precision.HIGHEST,
        preferred_element_type=jnp.float32,
    )
    rank_in = jnp.sum(before * onehot_table, axis=1).astype(jnp.int32)
    slot_index = (routed % per_group * group_count + routed // per_group) * slot_depth + rank_in
    slot_count = route_count * slot_depth
    placement = (jnp.arange(slot_count)[:, None] == slot_index[None, :]).astype(jnp.bfloat16)
    normed_assign = jnp.repeat(normed, TOP, axis=0)
    outgoing = jnp.dot(placement, normed_assign, preferred_element_type=jnp.float32).astype(
        jnp.bfloat16
    )
    outgoing = outgoing.reshape(route_count, slot_depth, D)
    incoming = lax.all_to_all(outgoing, ROUTE, split_axis=0, concat_axis=0, tiled=True)
    flat_rows = incoming.reshape(slot_count, D)

    summed = experts(flat_rows, quarter_weights)
    summed = summed.reshape(route_count, slot_depth, D)
    delivered = lax.all_to_all(summed, ROUTE, split_axis=0, concat_axis=0, tiled=True)
    expert_out = lax.dot_general(
        placement,
        delivered.reshape(slot_count, D),
        (((0,), (0,)), ((), ())),
        preferred_element_type=jnp.float32,
    )
    gated = expert_out.reshape(token_rows, TOP, D) * gate_values[0][:, :, None]
    layer_out = (mid_wide + jnp.sum(gated, axis=1)).astype(jnp.bfloat16)
    return layer_out[None]


def solution(mesh):
    ctx_size = mesh.shape["ctx"]
    exp_size = mesh.shape["exp"]
    split_mesh = Mesh(
        mesh.devices.reshape(ctx_size // QUARTERS, QUARTERS // 2, 2, exp_size),
        ("z", "yh", "yl", "e"),
    )
    rows = P("e", CTX, None)
    return jax.shard_map(
        layer,
        mesh=split_mesh,
        in_specs=(
            rows,
            rows,
            rows,
            rows,
            P(),
            rows,
            rows,
            P(CTX, "e", None, None, None),
            P(CTX, "e", None, None),
        ),
        out_specs=rows,
        check_vma=False,
    )
```

```python
import math

import jax
import jax.numpy as jnp
from jax import lax
from jax.experimental import pallas as pl
from jax.experimental.pallas import tpu as pltpu
from jax.sharding import Mesh
from jax.sharding import PartitionSpec as P

D = 2048
QUERY_HEADS = 16
KEY_VALUE_HEADS = 2
HEAD_SIZE = 128
TOP = 1
QUARTERS = 4

NEGATIVE_FILL = -1e30

CTX = ("z", "yh", "yl")
QUARTER_AXES = ("yh", "yl")
ROUTE = ("z", "e")


def attend_kernel(pos_ref, q_ref, k_ref, v_ref, res_ref, o_ref):
    rows_here = q_ref.shape[0]
    scores = lax.dot_general(
        q_ref[...], k_ref[...], (((1,), (1,)), ((), ())), preferred_element_type=jnp.float32
    ) / math.sqrt(HEAD_SIZE)
    query_pos = lax.broadcasted_iota(jnp.int32, scores.shape, 0) + pos_ref[0] * rows_here
    key_pos = lax.broadcasted_iota(jnp.int32, scores.shape, 1)
    scores = jnp.where(key_pos <= query_pos, scores, NEGATIVE_FILL)
    row_peak = jnp.max(scores, axis=1, keepdims=True)
    expo_vals = jnp.exp(scores - row_peak)
    row_total = jnp.sum(expo_vals, axis=1, keepdims=True)
    summed = jnp.dot(expo_vals.astype(jnp.bfloat16), v_ref[...], preferred_element_type=jnp.float32)
    o_ref[...] = (res_ref[...].astype(jnp.float32) + summed / row_total).astype(o_ref.dtype)


def attend(pos, queries, kv_all, residual_rows):
    rows_here = queries.shape[0]
    keys_all = kv_all.shape[0]
    per_kv = QUERY_HEADS // KEY_VALUE_HEADS
    flops = QUERY_HEADS * 4 * rows_here * keys_all * HEAD_SIZE
    grid_spec = pltpu.PrefetchScalarGridSpec(
        num_scalar_prefetch=1,
        grid=(QUERY_HEADS,),
        in_specs=[
            pl.BlockSpec((rows_here, HEAD_SIZE), lambda h, p: (0, h)),
            pl.BlockSpec((keys_all, HEAD_SIZE), lambda h, p: (0, h // per_kv)),
            pl.BlockSpec((keys_all, HEAD_SIZE), lambda h, p: (0, KEY_VALUE_HEADS + h // per_kv)),
            pl.BlockSpec((rows_here, HEAD_SIZE), lambda h, p: (0, h)),
        ],
        out_specs=pl.BlockSpec((rows_here, HEAD_SIZE), lambda h, p: (0, h)),
    )
    return pl.pallas_call(
        attend_kernel,
        out_shape=jax.ShapeDtypeStruct((rows_here, QUERY_HEADS * HEAD_SIZE), jnp.bfloat16),
        grid_spec=grid_spec,
        cost_estimate=pl.CostEstimate(
            flops=flops,
            transcendentals=QUERY_HEADS * rows_here * keys_all,
            bytes_accessed=2 * kv_all.size * 2 + queries.size * 2 + rows_here * D * 4,
        ),
    )(pos, queries, kv_all, kv_all, residual_rows)


def expert_kernel(rows_ref, w0_ref, w1_ref, w2_ref, w3_ref, o_ref, wbuf, sems):
    hid = w0_ref.shape[1]
    sources = (w0_ref, w1_ref, w2_ref, w3_ref)
    copies = [
        pltpu.make_async_copy(src, wbuf.at[i], sems.at[i]) for i, src in enumerate(sources)
    ]
    for copy in copies:
        copy.start()
    rows = rows_ref[...]
    total = None
    for i, copy in enumerate(copies):
        copy.wait()
        gate_up = wbuf[i, 0:2].reshape(2 * hid, rows.shape[1])
        projected = lax.dot_general(
            gate_up, rows, (((1,), (1,)), ((), ())), preferred_element_type=jnp.float32
        )
        gate, up = projected[:hid], projected[hid:]
        hidden = (gate / (1.0 + jnp.exp(-gate)) * up).astype(jnp.bfloat16)
        part_out = lax.dot_general(
            hidden, wbuf[i, 2], (((0,), (0,)), ((), ())), preferred_element_type=jnp.float32
        )
        part_out = part_out.astype(jnp.bfloat16).astype(jnp.float32)
        total = part_out if total is None else total + part_out
    o_ref[...] = total.astype(o_ref.dtype)


def experts(rows, quarter_weights):
    count, hid, width = quarter_weights[0].shape
    slots = rows.shape[0]
    return pl.pallas_call(
        expert_kernel,
        out_shape=jax.ShapeDtypeStruct((slots, width), jnp.bfloat16),
        in_specs=[pl.BlockSpec(memory_space=pltpu.VMEM)]
        + [pl.BlockSpec(memory_space=pl.ANY)] * len(quarter_weights),
        out_specs=pl.BlockSpec(memory_space=pltpu.VMEM),
        scratch_shapes=[
            pltpu.VMEM((len(quarter_weights), count, hid, width), jnp.bfloat16),
            pltpu.SemaphoreType.DMA((len(quarter_weights),)),
        ],
        compiler_params=pltpu.CompilerParams(vmem_limit_bytes=48 * 1024 * 1024),
        cost_estimate=pl.CostEstimate(
            flops=2 * slots * count * hid * width * len(quarter_weights),
            transcendentals=slots * hid * len(quarter_weights),
            bytes_accessed=2 * (count * hid * width * len(quarter_weights) + 2 * slots * width),
        ),
    )(rows, *quarter_weights)


def layer(
    queries,
    rotated_key_rows,
    value_row_array,
    residual,
    norm_gain,
    expert_ids,
    gate_values,
    w_gate_up,
    w_down,
):
    token_rows = queries.shape[1]
    route_count = lax.axis_size("z") * lax.axis_size("e")
    group_count = lax.axis_size("e")
    per_group = lax.axis_size("z")

    own_kv = jnp.concatenate([rotated_key_rows[0], value_row_array[0]], axis=-1)
    kv_pair = lax.all_gather(own_kv, "yh", axis=0, tiled=False)
    kv_all = lax.all_gather(kv_pair, "z", axis=0, tiled=False).reshape(-1, own_kv.shape[-1])

    quarter_count = lax.axis_size(QUARTER_AXES)
    own_weights = jnp.concatenate([w_gate_up[0, 0], w_down[0, 0][None]], axis=0)
    quarter_weights = [own_weights]
    for shift in range(1, quarter_count):
        pairs = [(q, (q + shift) % quarter_count) for q in range(quarter_count)]
        quarter_weights.append(lax.ppermute(own_weights, QUARTER_AXES, pairs))
    pos = (lax.axis_index("z") * lax.axis_size("yh") + lax.axis_index("yh")).astype(jnp.int32)
    mid_rows = attend(pos.reshape(1), queries[0], kv_all, residual[0])

    mid_wide = mid_rows.astype(jnp.float32)
    inverse = lax.rsqrt(jnp.mean(mid_wide * mid_wide, axis=-1, keepdims=True) + 1e-06)
    normed = (mid_wide * inverse * norm_gain).astype(jnp.bfloat16)

    slot_depth = max(2, 2 * token_rows * TOP // route_count)
    assign_count = token_rows * TOP
    routed = expert_ids[0].reshape(assign_count)
    onehot_table = (routed[:, None] == jnp.arange(route_count)[None, :]).astype(jnp.float32)
    earlier_blocks = (jnp.arange(assign_count)[:, None] > jnp.arange(assign_count)[None, :]).astype(
        jnp.float32
    )
    before = jnp.dot(
        earlier_blocks,
        onehot_table,
        precision=lax.Precision.HIGHEST,
        preferred_element_type=jnp.float32,
    )
    rank_in = jnp.sum(before * onehot_table, axis=1).astype(jnp.int32)
    slot_index = (routed % per_group * group_count + routed // per_group) * slot_depth + rank_in
    slot_count = route_count * slot_depth
    placement = (jnp.arange(slot_count)[:, None] == slot_index[None, :]).astype(jnp.bfloat16)
    normed_assign = jnp.repeat(normed, TOP, axis=0)
    outgoing = jnp.dot(placement, normed_assign, preferred_element_type=jnp.float32).astype(
        jnp.bfloat16
    )
    outgoing = outgoing.reshape(route_count, slot_depth, D)
    incoming = lax.all_to_all(outgoing, ROUTE, split_axis=0, concat_axis=0, tiled=True)
    flat_rows = incoming.reshape(slot_count, D)

    summed = experts(flat_rows, quarter_weights)
    summed = summed.reshape(route_count, slot_depth, D)
    delivered = lax.all_to_all(summed, ROUTE, split_axis=0, concat_axis=0, tiled=True)
    expert_out = lax.dot_general(
        placement,
        delivered.reshape(slot_count, D),
        (((0,), (0,)), ((), ())),
        preferred_element_type=jnp.float32,
    )
    gated = expert_out.reshape(token_rows, TOP, D) * gate_values[0][:, :, None]
    layer_out = (mid_wide + jnp.sum(gated, axis=1)).astype(jnp.bfloat16)
    return layer_out[None]


def solution(mesh):
    ctx_size = mesh.shape["ctx"]
    exp_size = mesh.shape["exp"]
    split_mesh = Mesh(
        mesh.devices.reshape(ctx_size // QUARTERS, QUARTERS // 2, 2, exp_size),
        ("z", "yh", "yl", "e"),
    )
    rows = P("e", CTX, None)
    return jax.shard_map(
        layer,
        mesh=split_mesh,
        in_specs=(
            rows,
            rows,
            rows,
            rows,
            P(),
            rows,
            rows,
            P(CTX, "e", None, None, None),
            P(CTX, "e", None, None),
        ),
        out_specs=rows,
        check_vma=False,
    )
```
